32 devices in a mesh: shot: 8 (over z, y), off: 4 (over x, core).
Axes of the slice: x: 2, y: 2, z: 4, core: 2. Of those that a mesh axis runs over, the one named last changes fastest.
Arguments:
- traces: float32 [8192, 2048], P(('shot', 'off')), may hold values from -6 to 6
- cmp_bin: int32 [8192], P(('shot', 'off')), may hold values from 0 to 255, as said below
- offset_class: int32 [8192], P(('shot', 'off')), may hold values from 0 to 79, as said below
- bin_rank: int32 [256], replicated, may hold values from 0 to 255, as said below
- filter_off: float32 [7], replicated, may hold values from -2.5 to 2.5
- filter_time: float32 [65], replicated, may hold values from -2 to 2
Outputs:
- planes: float32 [80, 2048, 256], P('off', 'shot')
The draws below stay inside these ranges and needn't reach their ends.
Inputs may be any that keep to these rules, and one draw needn't show every extreme that they name: `cmp_bin`: in each aligned block of 256 rows (the rows of one device) at most 128 rows name bins with the same owner bin_rank // 32; one owner, the same for all blocks, gets exactly 128 rows of every block, and every other owner gets a whole number of rows next to 128 / (7) (its floor or ceiling). `offset_class`: row r has a class from g * 20 to g * 20 + 19, with g = (r // 256) % 4. `bin_rank`: A permutation.
All inputs are finite; a program needn't handle non-finite values.
Results may differ from the reference program's by a relative error of at most 0.00007.
Values sent between devices are 32-bit elements; how exact they have to be, the bound alone decides.
No kernel may reach another device: no remote copies, remote signals or barrier semaphores. Data moves between devices by JAX's collectives and lax.ppermute only.
A program may use at most 128 MiB of HBM per device.

```python
import jax
import jax.numpy as jnp

NT = 2048
OFFC = 80
TR_DEV = 256
BOWN = 32
LAG_OFF = 3
LAG_T = 32
OFF_DEV = 20
BINS = 256
TRACES = 8192
CAP = 128


def survey_layout(key):
    ranking = jax.random.permutation(jax.random.fold_in(key, 101), BINS).astype(jnp.int32)
    ordering = jnp.argsort(ranking).astype(jnp.int32)
    owner_count = BINS // BOWN
    block_count = TRACES // TR_DEV
    busiest = jax.random.randint(jax.random.fold_in(key, 102), (), 0, owner_count)
    subkeys = jax.random.split(jax.random.fold_in(key, 103), block_count)
    placing = jax.vmap(lambda subkey: jax.random.permutation(subkey, TR_DEV))(subkeys).astype(jnp.int32)
    others = max(owner_count - 1, 1)
    owning = jnp.where(placing < CAP, busiest, (busiest + 1 + (placing - CAP) % others) % owner_count)
    slot_index = jax.random.randint(jax.random.fold_in(key, 104), (block_count, TR_DEV), 0, BOWN)
    position = (owning * BOWN + slot_index).reshape(-1)
    bin_ids = ordering[position]
    return (ranking, bin_ids.astype(jnp.int32))


def draw_cmp_bin(key, part):
    return survey_layout(key)[1]


def draw_bin_rank(key, part):
    return survey_layout(key)[0]


def draw_offset_class(key, part):
    row_index = jnp.arange(TRACES, dtype=jnp.int32)
    group_index = row_index // TR_DEV % (OFFC // OFF_DEV)
    within = jax.random.randint(jax.random.fold_in(key, 105), (TRACES,), 0, OFF_DEV)
    return (group_index * OFF_DEV + within).astype(jnp.int32)


def shard_levels(key, extent, cuts, smallest, top_value):
    def one(dim, shards_of):
        steps = jax.random.uniform(jax.random.fold_in(jax.random.fold_in(key, 6), dim), (shards_of,), jnp.float32, smallest / len(cuts), top_value / len(cuts))
        return jnp.repeat(jnp.exp(steps), extent[dim] // shards_of).reshape((-1,) + (1,) * (len(extent) - dim - 1))

    factor_of = one(*cuts[0])
    for cut in cuts[1:]:
        factor_of = factor_of * one(*cut)
    return factor_of


def bell_draw(own_key, extent, scale, limit, shards=(), kind=jnp.bfloat16):
    array = scale * jax.random.normal(own_key, extent, jnp.float32)
    if shards:
        array = array * shard_levels(own_key, extent, shards, -0.22, 0.18)
    return jnp.clip(array, -limit, limit).astype(kind)


def setup_inputs(seed: int = 0) -> dict:
    keys = jax.random.split(jax.random.key(seed), 7)
    traces = bell_draw(keys[0], (TRACES, NT), 1.0, 6.0, ((0, 32),), jnp.float32)
    cmp_bin = draw_cmp_bin(jax.random.fold_in(keys[6], 71), 0)
    offset_class = draw_offset_class(jax.random.fold_in(keys[6], 71), 0)
    bin_rank = draw_bin_rank(jax.random.fold_in(keys[6], 71), 0)
    filter_off = bell_draw(keys[4], (2 * LAG_OFF + 1,), 0.4, 2.5, (), jnp.float32)
    filter_time = bell_draw(keys[5], (2 * LAG_T + 1,), 0.125, 2.0, (), jnp.float32)
    return {"traces": traces, "cmp_bin": cmp_bin, "offset_class": offset_class, "bin_rank": bin_rank, "filter_off": filter_off, "filter_time": filter_time}


def reference(traces, cmp_bin, offset_class, bin_rank, filter_off, filter_time):
    cell_count = OFFC * BINS
    place = bin_rank[cmp_bin].astype(jnp.int32)
    cell_index = (offset_class * BINS + place).astype(jnp.int32)
    stacked = jax.ops.segment_sum(traces, cell_index, num_segments=cell_count)
    fold_count = jax.ops.segment_sum(jnp.ones(cell_index.shape, jnp.float32), cell_index, num_segments=cell_count)
    scaled = (stacked / jnp.maximum(fold_count, 1.0)[:, None]).reshape(OFFC, BINS, NT)
    padded = jnp.pad(scaled, ((LAG_OFF, LAG_OFF), (0, 0), (0, 0)))
    mixed = filter_off[0] * padded[0:OFFC]
    for offset_tap in range(1, 2 * LAG_OFF + 1):
        mixed = mixed + filter_off[offset_tap] * padded[offset_tap:offset_tap + OFFC]
    padded = jnp.pad(mixed, ((0, 0), (0, 0), (LAG_T, LAG_T)))
    filtered = filter_time[0] * padded[:, :, 0:NT]
    for time_tap in range(1, 2 * LAG_T + 1):
        filtered = filtered + filter_time[time_tap] * padded[:, :, time_tap:time_tap + NT]
    return jnp.transpose(filtered, (0, 2, 1))
```

```python
import jax
import jax.numpy as jnp
from jax import lax
from jax.sharding import PartitionSpec as P

OFFC = 80


def tap_table(filter_time, width_in, width_out):
    inner = jnp.arange(width_in, dtype=jnp.int32)[:, None]
    outer = jnp.arange(width_out, dtype=jnp.int32)[None, :]
    distance = inner - outer
    taps = jnp.arange(filter_time.shape[0], dtype=jnp.int32)
    matches = distance[:, :, None] == taps[None, None, :]
    return jnp.sum(jnp.where(matches, filter_time[None, None, :], 0.0), axis=2)


def block_filter(data, filter_time):
    reach = filter_time.shape[0] // 2
    block_width = 128
    leading = data.shape[:-1]
    samples = data.shape[-1]
    blocks = data.reshape(leading + (samples // block_width, block_width))
    zeroes = jnp.zeros(leading + (1, reach), jnp.float32)
    before = jnp.concatenate([zeroes, blocks[..., :-1, block_width - reach :]], axis=-2)
    after = jnp.concatenate([blocks[..., 1:, :reach], zeroes], axis=-2)
    extended = jnp.concatenate([before, blocks, after], axis=-1)
    table = tap_table(filter_time, block_width + 2 * reach, block_width)
    result = jnp.einsum("...ki,io->...ko", extended, table, precision=lax.Precision.HIGHEST)
    return result.reshape(leading + (samples,))


def class_halo(cells, reach):
    count = lax.axis_size("off")
    ends = count - 1
    head = cells[:reach]
    tail = cells[cells.shape[0] - reach :]
    before = lax.ppermute(tail, "off", [(i, i + 1) for i in range(ends)])
    after = lax.ppermute(head, "off", [(i + 1, i) for i in range(ends)])
    return jnp.concatenate([before, cells, after], axis=0)


def body(traces, cmp_bin, offset_class, bin_rank, filter_off, filter_time):
    shots = lax.axis_size("shot")
    off_dev = OFFC // lax.axis_size("off")
    first_class = lax.axis_index("off") * off_dev
    bin_count = bin_rank.shape[0]
    tr_dev, samples = traces.shape
    window = samples // shots
    cell_count = off_dev * bin_count

    filtered = block_filter(traces, filter_time)
    outgoing = jnp.transpose(filtered.reshape(tr_dev, shots, window), (1, 0, 2))
    received = lax.all_to_all(outgoing, "shot", 0, 0, tiled=True)
    received = received.reshape(shots * tr_dev, window)

    place = jnp.take(bin_rank, cmp_bin, axis=0)
    cell = (offset_class - first_class) * bin_count + place
    cells = lax.all_gather(cell, "shot", axis=0, tiled=True)

    fold = jax.ops.segment_sum(jnp.ones(cells.shape, jnp.float32), cells, num_segments=cell_count)
    scale = 1.0 / jnp.maximum(jnp.take(fold, cells, axis=0), 1.0)
    stacked = jax.ops.segment_sum(received * scale[:, None], cells, num_segments=cell_count)
    stacked = stacked.reshape(off_dev, bin_count, window)

    reach = filter_off.shape[0] // 2
    padded = class_halo(stacked, reach)
    mixed = filter_off[0] * padded[0:off_dev]
    for offset_tap in range(1, filter_off.shape[0]):
        mixed = mixed + filter_off[offset_tap] * padded[offset_tap : offset_tap + off_dev]
    return jnp.transpose(mixed, (0, 2, 1))


def solution(mesh):
    return jax.shard_map(
        body,
        mesh=mesh,
        in_specs=(P(("shot", "off"), None), P(("shot", "off")), P(("shot", "off")), P(), P(), P()),
        out_specs=P("off", "shot", None),
        check_vma=False,
    )
```

```python
import functools

import jax
import jax.numpy as jnp
from jax import lax
from jax.sharding import PartitionSpec as P
from jax.experimental import pallas as pl
from jax.experimental.pallas import tpu as pltpu

OFFC = 80


def tap_table(filter_time, width_in, width_out):
    inner = jnp.arange(width_in, dtype=jnp.int32)[:, None]
    outer = jnp.arange(width_out, dtype=jnp.int32)[None, :]
    distance = inner - outer
    taps = jnp.arange(filter_time.shape[0], dtype=jnp.int32)
    matches = distance[:, :, None] == taps[None, None, :]
    return jnp.sum(jnp.where(matches, filter_time[None, None, :], 0.0), axis=2)


def block_filter(data, filter_time):
    reach = filter_time.shape[0] // 2
    block_width = 128
    leading = data.shape[:-1]
    samples = data.shape[-1]
    blocks = data.reshape(leading + (samples // block_width, block_width))
    zeroes = jnp.zeros(leading + (1, reach), jnp.float32)
    before = jnp.concatenate([zeroes, blocks[..., :-1, block_width - reach :]], axis=-2)
    after = jnp.concatenate([blocks[..., 1:, :reach], zeroes], axis=-2)
    extended = jnp.concatenate([before, blocks, after], axis=-1)
    table = tap_table(filter_time, block_width + 2 * reach, block_width)
    result = jnp.einsum("...ki,io->...ko", extended, table, precision=lax.Precision.HIGHEST)
    return result.reshape(leading + (samples,))


def mix_kernel(taps, filter_ref, ext_ref, out_ref):
    c = pl.program_id(0)
    acc = filter_ref[0] * ext_ref[c]
    for k in range(1, taps):
        acc = acc + filter_ref[k] * ext_ref[c + k]
    out_ref[0] = acc.T


def offset_mix(ext, filter_off, count):
    taps = filter_off.shape[0]
    _, rows, cols = ext.shape
    if rows % 128 or cols % 128:
        mixed = filter_off[0] * ext[0:count]
        for k in range(1, taps):
            mixed = mixed + filter_off[k] * ext[k : k + count]
        return jnp.transpose(mixed, (0, 2, 1))
    return pl.pallas_call(
        functools.partial(mix_kernel, taps),
        grid=(count,),
        in_specs=[
            pl.BlockSpec(memory_space=pltpu.SMEM),
            pl.BlockSpec(memory_space=pltpu.VMEM),
        ],
        out_specs=pl.BlockSpec((1, cols, rows), lambda c: (c, 0, 0)),
        out_shape=jax.ShapeDtypeStruct((count, cols, rows), jnp.float32),
    )(filter_off, ext)


def body(traces, cmp_bin, offset_class, bin_rank, filter_off, filter_time):
    shots = lax.axis_size("shot")
    off_count = lax.axis_size("off")
    off_dev = OFFC // off_count
    first_class = lax.axis_index("off") * off_dev
    bin_count = bin_rank.shape[0]
    tr_dev, samples = traces.shape
    window = samples // shots
    reach = filter_off.shape[0] // 2
    ext_classes = off_dev + 2 * reach

    place = jnp.take(bin_rank, cmp_bin, axis=0)
    cell = (offset_class - first_class + reach) * bin_count + place
    label_rows = -(-tr_dev // window)
    labels = jnp.pad(cell.astype(jnp.float32), (0, label_rows * window - tr_dev))
    labels = jnp.broadcast_to(labels.reshape(1, label_rows, window), (shots, label_rows, window))

    filtered = block_filter(traces, filter_time)
    outgoing = jnp.transpose(filtered.reshape(tr_dev, shots, window), (1, 0, 2))
    outgoing = jnp.concatenate([outgoing, labels], axis=1)
    received = lax.all_to_all(outgoing, "shot", 0, 0, tiled=True)
    rows = received[:, :tr_dev].reshape(shots * tr_dev, window)
    cells = received[:, tr_dev:].reshape(shots, label_rows * window)[:, :tr_dev]
    cells = cells.reshape(shots * tr_dev).astype(jnp.int32)

    fold = jnp.sum((cells[:, None] == cells[None, :]).astype(jnp.float32), axis=1)
    scale = 1.0 / jnp.maximum(fold, 1.0)
    stacked = jax.ops.segment_sum(rows * scale[:, None], cells, num_segments=ext_classes * bin_count)
    stacked = stacked.reshape(ext_classes, bin_count, window)

    ends = off_count - 1
    head = stacked[reach : 2 * reach]
    tail = stacked[off_dev : off_dev + reach]
    before = lax.ppermute(tail, "off", [(i, i + 1) for i in range(ends)])
    after = lax.ppermute(head, "off", [(i + 1, i) for i in range(ends)])
    ext = lax.dynamic_update_slice_in_dim(stacked, before, 0, axis=0)
    ext = lax.dynamic_update_slice_in_dim(ext, after, off_dev + reach, axis=0)
    return offset_mix(ext, filter_off, off_dev)


def solution(mesh):
    return jax.shard_map(
        body,
        mesh=mesh,
        in_specs=(P(("shot", "off"), None), P(("shot", "off")), P(("shot", "off")), P(), P(), P()),
        out_specs=P("off", "shot", None),
        check_vma=False,
    )
```

```python
import functools

import jax
import jax.numpy as jnp
from jax import lax
from jax.sharding import PartitionSpec as P
from jax.experimental import pallas as pl
from jax.experimental.pallas import tpu as pltpu

OFFC = 80


def tap_table(filter_time, width_in, width_out):
    inner = jnp.arange(width_in, dtype=jnp.int32)[:, None]
    outer = jnp.arange(width_out, dtype=jnp.int32)[None, :]
    distance = inner - outer
    taps = jnp.arange(filter_time.shape[0], dtype=jnp.int32)
    matches = distance[:, :, None] == taps[None, None, :]
    return jnp.sum(jnp.where(matches, filter_time[None, None, :], 0.0), axis=2)


def block_filter(data, filter_time):
    reach = filter_time.shape[0] // 2
    block_width = 128
    leading = data.shape[:-1]
    samples = data.shape[-1]
    blocks = data.reshape(leading + (samples // block_width, block_width))
    zeroes = jnp.zeros(leading + (1, reach), jnp.float32)
    before = jnp.concatenate([zeroes, blocks[..., :-1, block_width - reach :]], axis=-2)
    after = jnp.concatenate([blocks[..., 1:, :reach], zeroes], axis=-2)
    extended = jnp.concatenate([before, blocks, after], axis=-1)
    table = tap_table(filter_time, block_width + 2 * reach, block_width)
    result = jnp.einsum("...ki,io->...ko", extended, table, precision=lax.Precision.HIGHEST)
    return result.reshape(leading + (samples,))


def mix_kernel(taps, count, filter_ref, ext_ref, out_ref):
    for c in range(count):
        acc = filter_ref[0] * ext_ref[c]
        for k in range(1, taps):
            acc = acc + filter_ref[k] * ext_ref[c + k]
        out_ref[c] = acc.T


def offset_mix(ext, filter_off, count):
    taps = filter_off.shape[0]
    classes, rows, cols = ext.shape
    if rows % 128 or cols % 128:
        mixed = filter_off[0] * ext[0:count]
        for k in range(1, taps):
            mixed = mixed + filter_off[k] * ext[k : k + count]
        return jnp.transpose(mixed, (0, 2, 1))
    tile = 128
    return pl.pallas_call(
        functools.partial(mix_kernel, taps, count),
        grid=(rows // tile, cols // tile),
        in_specs=[
            pl.BlockSpec(memory_space=pltpu.SMEM),
            pl.BlockSpec((classes, tile, tile), lambda i, j: (0, i, j)),
        ],
        out_specs=pl.BlockSpec((count, tile, tile), lambda i, j: (0, j, i)),
        out_shape=jax.ShapeDtypeStruct((count, cols, rows), jnp.float32),
    )(filter_off, ext)


def body(traces, cmp_bin, offset_class, bin_rank, filter_off, filter_time):
    shots = lax.axis_size("shot")
    off_count = lax.axis_size("off")
    off_dev = OFFC // off_count
    first_class = lax.axis_index("off") * off_dev
    bin_count = bin_rank.shape[0]
    tr_dev, samples = traces.shape
    window = samples // shots
    reach = filter_off.shape[0] // 2
    ext_classes = off_dev + 2 * reach
    halves = 2 if tr_dev % 16 == 0 else 1
    part = tr_dev // halves

    place = jnp.take(bin_rank, cmp_bin, axis=0)
    cell = (offset_class - first_class + reach) * bin_count + place
    label_rows = -(-tr_dev // window)
    labels = jnp.pad(cell.astype(jnp.float32), (0, label_rows * window - tr_dev))
    labels = jnp.broadcast_to(labels.reshape(1, label_rows, window), (shots, label_rows, window))

    pieces = []
    for h in range(halves):
        filtered = block_filter(traces[h * part : (h + 1) * part], filter_time)
        outgoing = jnp.transpose(filtered.reshape(part, shots, window), (1, 0, 2))
        if h == 0:
            outgoing = jnp.concatenate([outgoing, labels], axis=1)
        pieces.append(lax.all_to_all(outgoing, "shot", 0, 0, tiled=True))
    cells = pieces[0][:, part:].reshape(shots, label_rows * window)[:, :tr_dev]
    cells = cells.astype(jnp.int32)
    flat = cells.reshape(shots * tr_dev)
    fold = jnp.sum((flat[:, None] == flat[None, :]).astype(jnp.float32), axis=1)
    scale = (1.0 / jnp.maximum(fold, 1.0)).reshape(shots, tr_dev)

    stacked = jnp.zeros((ext_classes * bin_count, window), jnp.float32)
    for h in range(halves):
        rows = pieces[h][:, :part] * scale[:, h * part : (h + 1) * part, None]
        index = cells[:, h * part : (h + 1) * part].reshape(shots * part)
        stacked = stacked.at[index].add(rows.reshape(shots * part, window))
    stacked = stacked.reshape(ext_classes, bin_count, window)

    ends = off_count - 1
    head = stacked[reach : 2 * reach]
    tail = stacked[off_dev : off_dev + reach]
    before = lax.ppermute(tail, "off", [(i, i + 1) for i in range(ends)])
    after = lax.ppermute(head, "off", [(i + 1, i) for i in range(ends)])
    ext = lax.dynamic_update_slice_in_dim(stacked, before, 0, axis=0)
    ext = lax.dynamic_update_slice_in_dim(ext, after, off_dev + reach, axis=0)
    return offset_mix(ext, filter_off, off_dev)


def solution(mesh):
    return jax.shard_map(
        body,
        mesh=mesh,
        in_specs=(P(("shot", "off"), None), P(("shot", "off")), P(("shot", "off")), P(), P(), P()),
        out_specs=P("off", "shot", None),
        check_vma=False,
    )
```

```python
import functools

import jax
import jax.numpy as jnp
from jax import lax
from jax.sharding import PartitionSpec as P
from jax.experimental import pallas as pl
from jax.experimental.pallas import tpu as pltpu

OFFC = 80


def tap_table(filter_time, width_in, width_out):
    inner = jnp.arange(width_in, dtype=jnp.int32)[:, None]
    outer = jnp.arange(width_out, dtype=jnp.int32)[None, :]
    distance = inner - outer
    taps = jnp.arange(filter_time.shape[0], dtype=jnp.int32)
    matches = distance[:, :, None] == taps[None, None, :]
    return jnp.sum(jnp.where(matches, filter_time[None, None, :], 0.0), axis=2)


def block_filter(data, filter_time):
    reach = filter_time.shape[0] // 2
    block_width = 128
    leading = data.shape[:-1]
    samples = data.shape[-1]
    blocks = data.reshape(leading + (samples // block_width, block_width))
    zeroes = jnp.zeros(leading + (1, reach), jnp.float32)
    before = jnp.concatenate([zeroes, blocks[..., :-1, block_width - reach :]], axis=-2)
    after = jnp.concatenate([blocks[..., 1:, :reach], zeroes], axis=-2)
    extended = jnp.concatenate([before, blocks, after], axis=-1)
    table = tap_table(filter_time, block_width + 2 * reach, block_width)
    result = jnp.einsum("...ki,io->...ko", extended, table, precision=lax.Precision.HIGHEST)
    return result.reshape(leading + (samples,))


def mix_kernel(taps, count, filter_ref, ext_ref, out_ref):
    for c in range(count):
        acc = filter_ref[0] * ext_ref[c]
        for k in range(1, taps):
            acc = acc + filter_ref[k] * ext_ref[c + k]
        out_ref[c] = acc.T


def offset_mix(ext, filter_off, count):
    taps = filter_off.shape[0]
    classes, rows, cols = ext.shape
    if rows % 128 or cols % 128:
        mixed = filter_off[0] * ext[0:count]
        for k in range(1, taps):
            mixed = mixed + filter_off[k] * ext[k : k + count]
        return jnp.transpose(mixed, (0, 2, 1))
    tile = 128
    return pl.pallas_call(
        functools.partial(mix_kernel, taps, count),
        grid=(rows // tile, cols // tile),
        in_specs=[
            pl.BlockSpec(memory_space=pltpu.SMEM),
            pl.BlockSpec((classes, tile, tile), lambda i, j: (0, i, j)),
        ],
        out_specs=pl.BlockSpec((count, tile, tile), lambda i, j: (0, j, i)),
        out_shape=jax.ShapeDtypeStruct((count, cols, rows), jnp.float32),
    )(filter_off, ext)


def scatter_kernel(count, cell_ref, scale_ref, rows_ref, out_ref):
    out_ref[...] = jnp.zeros(out_ref.shape, jnp.float32)

    def step(r, carry):
        x = cell_ref[r]
        out_ref[pl.ds(x, 1), :] += rows_ref[pl.ds(r, 1), :] * scale_ref[r]
        return carry

    lax.fori_loop(0, count, step, 0, unroll=8)


def stack_rows(rows, cells, scale, segments):
    count, width = rows.shape
    if width % 128:
        return jax.ops.segment_sum(rows * scale[:, None], cells, num_segments=segments)
    return pl.pallas_call(
        functools.partial(scatter_kernel, count),
        in_specs=[
            pl.BlockSpec(memory_space=pltpu.SMEM),
            pl.BlockSpec(memory_space=pltpu.SMEM),
            pl.BlockSpec(memory_space=pltpu.VMEM),
        ],
        out_specs=pl.BlockSpec(memory_space=pltpu.VMEM),
        out_shape=jax.ShapeDtypeStruct((segments, width), jnp.float32),
    )(cells, scale, rows)


def body(traces, cmp_bin, offset_class, bin_rank, filter_off, filter_time):
    shots = lax.axis_size("shot")
    off_count = lax.axis_size("off")
    off_dev = OFFC // off_count
    first_class = lax.axis_index("off") * off_dev
    bin_count = bin_rank.shape[0]
    tr_dev, samples = traces.shape
    window = samples // shots
    reach = filter_off.shape[0] // 2
    ext_classes = off_dev + 2 * reach

    matches = cmp_bin[:, None] == jnp.arange(bin_count, dtype=jnp.int32)[None, :]
    place = jnp.sum(jnp.where(matches, bin_rank[None, :], 0), axis=1)
    cell = (offset_class - first_class + reach) * bin_count + place
    label_rows = -(-tr_dev // window)
    labels = jnp.pad(cell.astype(jnp.float32), (0, label_rows * window - tr_dev))
    labels = jnp.broadcast_to(labels.reshape(1, label_rows, window), (shots, label_rows, window))

    filtered = block_filter(traces, filter_time)
    outgoing = jnp.transpose(filtered.reshape(tr_dev, shots, window), (1, 0, 2))
    outgoing = jnp.concatenate([outgoing, labels], axis=1)
    received = lax.all_to_all(outgoing, "shot", 0, 0, tiled=True)
    rows = received[:, :tr_dev].reshape(shots * tr_dev, window)
    cells = received[:, tr_dev:].reshape(shots, label_rows * window)[:, :tr_dev]
    cells = cells.reshape(shots * tr_dev).astype(jnp.int32)

    fold = jnp.sum((cells[:, None] == cells[None, :]).astype(jnp.float32), axis=1)
    scale = 1.0 / jnp.maximum(fold, 1.0)
    stacked = stack_rows(rows, cells, scale, ext_classes * bin_count)
    stacked = stacked.reshape(ext_classes, bin_count, window)

    ends = off_count - 1
    head = stacked[reach : 2 * reach]
    tail = stacked[off_dev : off_dev + reach]
    before = lax.ppermute(tail, "off", [(i, i + 1) for i in range(ends)])
    after = lax.ppermute(head, "off", [(i + 1, i) for i in range(ends)])
    ext = lax.dynamic_update_slice_in_dim(stacked, before, 0, axis=0)
    ext = lax.dynamic_update_slice_in_dim(ext, after, off_dev + reach, axis=0)
    return offset_mix(ext, filter_off, off_dev)


def solution(mesh):
    return jax.shard_map(
        body,
        mesh=mesh,
        in_specs=(P(("shot", "off"), None), P(("shot", "off")), P(("shot", "off")), P(), P(), P()),
        out_specs=P("off", "shot", None),
        check_vma=False,
    )
```

```python
import functools

import jax
import jax.numpy as jnp
from jax import lax
from jax.sharding import PartitionSpec as P
from jax.experimental import pallas as pl
from jax.experimental.pallas import tpu as pltpu

OFFC = 80


def tap_table(filter_time, width_in, width_out):
    inner = jnp.arange(width_in, dtype=jnp.int32)[:, None]
    outer = jnp.arange(width_out, dtype=jnp.int32)[None, :]
    distance = inner - outer
    taps = jnp.arange(filter_time.shape[0], dtype=jnp.int32)
    matches = distance[:, :, None] == taps[None, None, :]
    return jnp.sum(jnp.where(matches, filter_time[None, None, :], 0.0), axis=2)


def block_filter(data, filter_time):
    reach = filter_time.shape[0] // 2
    block_width = 128
    leading = data.shape[:-1]
    samples = data.shape[-1]
    blocks = data.reshape(leading + (samples // block_width, block_width))
    zeroes = jnp.zeros(leading + (1, reach), jnp.float32)
    before = jnp.concatenate([zeroes, blocks[..., :-1, block_width - reach :]], axis=-2)
    after = jnp.concatenate([blocks[..., 1:, :reach], zeroes], axis=-2)
    extended = jnp.concatenate([before, blocks, after], axis=-1)
    table = tap_table(filter_time, block_width + 2 * reach, block_width)
    result = jnp.einsum("...ki,io->...ko", extended, table, precision=lax.Precision.HIGHEST)
    return result.reshape(leading + (samples,))


def mix_kernel(taps, count, filter_ref, ext_ref, out_ref):
    for c in range(count):
        acc = filter_ref[0] * ext_ref[c]
        for k in range(1, taps):
            acc = acc + filter_ref[k] * ext_ref[c + k]
        out_ref[c] = acc.T


def offset_mix(ext, filter_off, count):
    taps = filter_off.shape[0]
    classes, rows, cols = ext.shape
    if rows % 128 or cols % 128:
        mixed = filter_off[0] * ext[0:count]
        for k in range(1, taps):
            mixed = mixed + filter_off[k] * ext[k : k + count]
        return jnp.transpose(mixed, (0, 2, 1))
    tile = 128
    return pl.pallas_call(
        functools.partial(mix_kernel, taps, count),
        grid=(rows // tile, cols // tile),
        in_specs=[
            pl.BlockSpec(memory_space=pltpu.SMEM),
            pl.BlockSpec((classes, tile, tile), lambda i, j: (0, i, j)),
        ],
        out_specs=pl.BlockSpec((count, tile, tile), lambda i, j: (0, j, i)),
        out_shape=jax.ShapeDtypeStruct((count, cols, rows), jnp.float32),
    )(filter_off, ext)


def scatter_kernel(lanes, shots, tr_dev, base, cell_ref, scale_ref, rows_ref, out_ref, *accs):
    segments = out_ref.shape[0]
    span = accs[0].shape[0]
    for acc in accs:
        acc[...] = jnp.zeros(acc.shape, jnp.float32)

    def step(i, carry):
        for k, acc in enumerate(accs):
            r = i * lanes + k
            x = cell_ref[r] - base
            src = r // tr_dev
            row = rows_ref[src, pl.ds(r - src * tr_dev, 1), :]
            acc[pl.ds(x, 1), :] += row * scale_ref[r]
        return carry

    lax.fori_loop(0, shots * tr_dev // lanes, step, 0, unroll=2)
    total = accs[0][...]
    for acc in accs[1:]:
        total = total + acc[...]
    out_ref[pl.ds(base, span), :] = total
    out_ref[pl.ds(0, base), :] = jnp.zeros((base, out_ref.shape[1]), jnp.float32)
    tail = segments - base - span
    out_ref[pl.ds(base + span, tail), :] = jnp.zeros((tail, out_ref.shape[1]), jnp.float32)


def stack_rows(received, cells, scale, base, span, segments):
    shots, _, width = received.shape
    count = cells.shape[0]
    tr_dev = count // shots
    lanes = 4
    if width % 128 or count % lanes or base % 8 or span % 8:
        rows = received[:, :tr_dev].reshape(count, width)
        return jax.ops.segment_sum(rows * scale[:, None], cells, num_segments=segments)
    return pl.pallas_call(
        functools.partial(scatter_kernel, lanes, shots, tr_dev, base),
        in_specs=[
            pl.BlockSpec(memory_space=pltpu.SMEM),
            pl.BlockSpec(memory_space=pltpu.SMEM),
            pl.BlockSpec(memory_space=pltpu.VMEM),
        ],
        out_specs=pl.BlockSpec(memory_space=pltpu.VMEM),
        out_shape=jax.ShapeDtypeStruct((segments, width), jnp.float32),
        scratch_shapes=[pltpu.VMEM((span, width), jnp.float32) for _ in range(lanes)],
        compiler_params=pltpu.CompilerParams(vmem_limit_bytes=60 * 1024 * 1024),
    )(cells, scale, received)


def body(traces, cmp_bin, offset_class, bin_rank, filter_off, filter_time):
    shots = lax.axis_size("shot")
    off_count = lax.axis_size("off")
    off_dev = OFFC // off_count
    first_class = lax.axis_index("off") * off_dev
    bin_count = bin_rank.shape[0]
    tr_dev, samples = traces.shape
    window = samples // shots
    reach = filter_off.shape[0] // 2
    ext_classes = off_dev + 2 * reach

    matches = cmp_bin[:, None] == jnp.arange(bin_count, dtype=jnp.int32)[None, :]
    place = jnp.sum(jnp.where(matches, bin_rank[None, :], 0), axis=1)
    cell = (offset_class - first_class + reach) * bin_count + place
    label_rows = -(-tr_dev // window)
    labels = jnp.pad(cell.astype(jnp.float32), (0, label_rows * window - tr_dev))
    labels = jnp.broadcast_to(labels.reshape(1, label_rows, window), (shots, label_rows, window))

    filtered = block_filter(traces, filter_time)
    outgoing = jnp.transpose(filtered.reshape(tr_dev, shots, window), (1, 0, 2))
    outgoing = jnp.concatenate([outgoing, labels], axis=1)
    received = lax.all_to_all(outgoing, "shot", 0, 0, tiled=True)
    cells = received[:, tr_dev:].reshape(shots, label_rows * window)[:, :tr_dev]
    cells = cells.reshape(shots * tr_dev).astype(jnp.int32)

    fold = jnp.sum((cells[:, None] == cells[None, :]).astype(jnp.float32), axis=1)
    scale = 1.0 / jnp.maximum(fold, 1.0)
    stacked = stack_rows(received, cells, scale, reach * bin_count, off_dev * bin_count, ext_classes * bin_count)
    stacked = stacked.reshape(ext_classes, bin_count, window)

    ends = off_count - 1
    head = stacked[reach : 2 * reach]
    tail = stacked[off_dev : off_dev + reach]
    before = lax.ppermute(tail, "off", [(i, i + 1) for i in range(ends)])
    after = lax.ppermute(head, "off", [(i + 1, i) for i in range(ends)])
    ext = lax.dynamic_update_slice_in_dim(stacked, before, 0, axis=0)
    ext = lax.dynamic_update_slice_in_dim(ext, after, off_dev + reach, axis=0)
    return offset_mix(ext, filter_off, off_dev)


def solution(mesh):
    return jax.shard_map(
        body,
        mesh=mesh,
        in_specs=(P(("shot", "off"), None), P(("shot", "off")), P(("shot", "off")), P(), P(), P()),
        out_specs=P("off", "shot", None),
        check_vma=False,
    )
```

```python
import functools

import jax
import jax.numpy as jnp
from jax import lax
from jax.sharding import PartitionSpec as P
from jax.experimental import pallas as pl
from jax.experimental.pallas import tpu as pltpu

OFFC = 80


def tap_table(filter_time, width_in, width_out):
    inner = jnp.arange(width_in, dtype=jnp.int32)[:, None]
    outer = jnp.arange(width_out, dtype=jnp.int32)[None, :]
    distance = inner - outer
    taps = jnp.arange(filter_time.shape[0], dtype=jnp.int32)
    matches = distance[:, :, None] == taps[None, None, :]
    return jnp.sum(jnp.where(matches, filter_time[None, None, :], 0.0), axis=2)


def block_filter(data, filter_time):
    reach = filter_time.shape[0] // 2
    block_width = 128
    leading = data.shape[:-1]
    samples = data.shape[-1]
    blocks = data.reshape(leading + (samples // block_width, block_width))
    zeroes = jnp.zeros(leading + (1, reach), jnp.float32)
    before = jnp.concatenate([zeroes, blocks[..., :-1, block_width - reach :]], axis=-2)
    after = jnp.concatenate([blocks[..., 1:, :reach], zeroes], axis=-2)
    extended = jnp.concatenate([before, blocks, after], axis=-1)
    table = tap_table(filter_time, block_width + 2 * reach, block_width)
    result = jnp.einsum("...ki,io->...ko", extended, table, precision=lax.Precision.HIGHEST)
    return result.reshape(leading + (samples,))


def mix_kernel(taps, count, filter_ref, ext_ref, out_ref):
    for c in range(count):
        acc = filter_ref[0] * ext_ref[c]
        for k in range(1, taps):
            acc = acc + filter_ref[k] * ext_ref[c + k]
        out_ref[c] = acc.T


def offset_mix(ext, filter_off, count):
    taps = filter_off.shape[0]
    classes, rows, cols = ext.shape
    if rows % 128 or cols % 128:
        mixed = filter_off[0] * ext[0:count]
        for k in range(1, taps):
            mixed = mixed + filter_off[k] * ext[k : k + count]
        return jnp.transpose(mixed, (0, 2, 1))
    tile = 128
    return pl.pallas_call(
        functools.partial(mix_kernel, taps, count),
        grid=(rows // tile, cols // tile),
        in_specs=[
            pl.BlockSpec(memory_space=pltpu.SMEM),
            pl.BlockSpec((classes, tile, tile), lambda i, j: (0, i, j)),
        ],
        out_specs=pl.BlockSpec((count, tile, tile), lambda i, j: (0, j, i)),
        out_shape=jax.ShapeDtypeStruct((count, cols, rows), jnp.float32),
    )(filter_off, ext)


def scatter_kernel(count, cell_ref, scale_ref, rows_ref, out_ref):
    out_ref[...] = jnp.zeros(out_ref.shape, jnp.float32)

    def step(i, carry):
        start = pl.multiple_of(i * 8, 8)
        tile = rows_ref[pl.ds(start, 8), :]
        for k in range(8):
            x = cell_ref[start + k]
            out_ref[pl.ds(x, 1), :] += tile[k : k + 1, :] * scale_ref[start + k]
        return carry

    lax.fori_loop(0, count // 8, step, 0)


def stack_rows(rows, cells, scale, segments):
    count, width = rows.shape
    if width % 128 or count % 8:
        return jax.ops.segment_sum(rows * scale[:, None], cells, num_segments=segments)
    return pl.pallas_call(
        functools.partial(scatter_kernel, count),
        in_specs=[
            pl.BlockSpec(memory_space=pltpu.SMEM),
            pl.BlockSpec(memory_space=pltpu.SMEM),
            pl.BlockSpec(memory_space=pltpu.VMEM),
        ],
        out_specs=pl.BlockSpec(memory_space=pltpu.VMEM),
        out_shape=jax.ShapeDtypeStruct((segments, width), jnp.float32),
    )(cells, scale, rows)


def body(traces, cmp_bin, offset_class, bin_rank, filter_off, filter_time):
    shots = lax.axis_size("shot")
    off_count = lax.axis_size("off")
    off_dev = OFFC // off_count
    first_class = lax.axis_index("off") * off_dev
    bin_count = bin_rank.shape[0]
    tr_dev, samples = traces.shape
    window = samples // shots
    reach = filter_off.shape[0] // 2
    ext_classes = off_dev + 2 * reach

    matches = cmp_bin[:, None] == jnp.arange(bin_count, dtype=jnp.int32)[None, :]
    place = jnp.sum(jnp.where(matches, bin_rank[None, :], 0), axis=1)
    cell = (offset_class - first_class + reach) * bin_count + place
    label_rows = -(-tr_dev // window)
    labels = jnp.pad(cell.astype(jnp.float32), (0, label_rows * window - tr_dev))
    labels = jnp.broadcast_to(labels.reshape(1, label_rows, window), (shots, label_rows, window))

    filtered = block_filter(traces, filter_time)
    outgoing = jnp.transpose(filtered.reshape(tr_dev, shots, window), (1, 0, 2))
    outgoing = jnp.concatenate([outgoing, labels], axis=1)
    received = lax.all_to_all(outgoing, "shot", 0, 0, tiled=True)
    rows = received[:, :tr_dev].reshape(shots * tr_dev, window)
    cells = received[:, tr_dev:].reshape(shots, label_rows * window)[:, :tr_dev]
    cells = cells.reshape(shots * tr_dev).astype(jnp.int32)

    fold = jnp.sum((cells[:, None] == cells[None, :]).astype(jnp.float32), axis=1)
    scale = 1.0 / jnp.maximum(fold, 1.0)
    stacked = stack_rows(rows, cells, scale, ext_classes * bin_count)
    stacked = stacked.reshape(ext_classes, bin_count, window)

    ends = off_count - 1
    head = stacked[reach : 2 * reach]
    tail = stacked[off_dev : off_dev + reach]
    before = lax.ppermute(tail, "off", [(i, i + 1) for i in range(ends)])
    after = lax.ppermute(head, "off", [(i + 1, i) for i in range(ends)])
    ext = lax.dynamic_update_slice_in_dim(stacked, before, 0, axis=0)
    ext = lax.dynamic_update_slice_in_dim(ext, after, off_dev + reach, axis=0)
    return offset_mix(ext, filter_off, off_dev)


def solution(mesh):
    return jax.shard_map(
        body,
        mesh=mesh,
        in_specs=(P(("shot", "off"), None), P(("shot", "off")), P(("shot", "off")), P(), P(), P()),
        out_specs=P("off", "shot", None),
        check_vma=False,
    )
```

```python
import functools

import jax
import jax.numpy as jnp
from jax import lax
from jax.sharding import PartitionSpec as P
from jax.experimental import pallas as pl
from jax.experimental.pallas import tpu as pltpu

OFFC = 80


def tap_table(filter_time, width_in, width_out):
    inner = jnp.arange(width_in, dtype=jnp.int32)[:, None]
    outer = jnp.arange(width_out, dtype=jnp.int32)[None, :]
    distance = inner - outer
    taps = jnp.arange(filter_time.shape[0], dtype=jnp.int32)
    matches = distance[:, :, None] == taps[None, None, :]
    return jnp.sum(jnp.where(matches, filter_time[None, None, :], 0.0), axis=2)


def block_filter(data, filter_time):
    reach = filter_time.shape[0] // 2
    block_width = 128
    leading = data.shape[:-1]
    samples = data.shape[-1]
    blocks = data.reshape(leading + (samples // block_width, block_width))
    zeroes = jnp.zeros(leading + (1, reach), jnp.float32)
    before = jnp.concatenate([zeroes, blocks[..., :-1, block_width - reach :]], axis=-2)
    after = jnp.concatenate([blocks[..., 1:, :reach], zeroes], axis=-2)
    extended = jnp.concatenate([before, blocks, after], axis=-1)
    table = tap_table(filter_time, block_width + 2 * reach, block_width)
    result = jnp.einsum("...ki,io->...ko", extended, table, precision=lax.Precision.HIGHEST)
    return result.reshape(leading + (samples,))


def mix_kernel(taps, count, reach, filter_ref, before_ref, own_ref, after_ref, out_ref):
    def plane(e):
        if e < reach:
            return before_ref[e]
        if e < reach + count:
            return own_ref[e - reach]
        return after_ref[e - reach - count]

    for c in range(count):
        acc = filter_ref[0] * plane(c)
        for k in range(1, taps):
            acc = acc + filter_ref[k] * plane(c + k)
        out_ref[c] = acc.T


def offset_mix(before, own, after, filter_off):
    taps = filter_off.shape[0]
    count, rows, cols = own.shape
    reach = before.shape[0]
    if rows % 128 or cols % 128:
        ext = jnp.concatenate([before, own, after], axis=0)
        mixed = filter_off[0] * ext[0:count]
        for k in range(1, taps):
            mixed = mixed + filter_off[k] * ext[k : k + count]
        return jnp.transpose(mixed, (0, 2, 1))
    tile = 128
    return pl.pallas_call(
        functools.partial(mix_kernel, taps, count, reach),
        grid=(rows // tile, cols // tile),
        in_specs=[
            pl.BlockSpec(memory_space=pltpu.SMEM),
            pl.BlockSpec((reach, tile, tile), lambda i, j: (0, i, j)),
            pl.BlockSpec((count, tile, tile), lambda i, j: (0, i, j)),
            pl.BlockSpec((reach, tile, tile), lambda i, j: (0, i, j)),
        ],
        out_specs=pl.BlockSpec((count, tile, tile), lambda i, j: (0, j, i)),
        out_shape=jax.ShapeDtypeStruct((count, cols, rows), jnp.float32),
    )(filter_off, before, own, after)


def scatter_kernel(count, cell_ref, scale_ref, rows_ref, out_ref):
    out_ref[...] = jnp.zeros(out_ref.shape, jnp.float32)

    def step(i, carry):
        start = pl.multiple_of(i * 8, 8)
        tile = rows_ref[pl.ds(start, 8), :]
        for k in range(8):
            x = cell_ref[start + k]
            out_ref[pl.ds(x, 1), :] += tile[k : k + 1, :] * scale_ref[start + k]
        return carry

    lax.fori_loop(0, count // 8, step, 0)


def stack_rows(rows, cells, scale, segments):
    count, width = rows.shape
    if width % 128 or count % 8:
        return jax.ops.segment_sum(rows * scale[:, None], cells, num_segments=segments)
    return pl.pallas_call(
        functools.partial(scatter_kernel, count),
        in_specs=[
            pl.BlockSpec(memory_space=pltpu.SMEM),
            pl.BlockSpec(memory_space=pltpu.SMEM),
            pl.BlockSpec(memory_space=pltpu.VMEM),
        ],
        out_specs=pl.BlockSpec(memory_space=pltpu.VMEM),
        out_shape=jax.ShapeDtypeStruct((segments, width), jnp.float32),
    )(cells, scale, rows)


def body(traces, cmp_bin, offset_class, bin_rank, filter_off, filter_time):
    shots = lax.axis_size("shot")
    off_count = lax.axis_size("off")
    off_dev = OFFC // off_count
    first_class = lax.axis_index("off") * off_dev
    bin_count = bin_rank.shape[0]
    tr_dev, samples = traces.shape
    window = samples // shots
    reach = filter_off.shape[0] // 2

    matches = cmp_bin[:, None] == jnp.arange(bin_count, dtype=jnp.int32)[None, :]
    place = jnp.sum(jnp.where(matches, bin_rank[None, :], 0), axis=1)
    cell = (offset_class - first_class) * bin_count + place
    label_rows = -(-tr_dev // window)
    labels = jnp.pad(cell.astype(jnp.float32), (0, label_rows * window - tr_dev))
    labels = jnp.broadcast_to(labels.reshape(1, label_rows, window), (shots, label_rows, window))

    filtered = block_filter(traces, filter_time)
    outgoing = jnp.transpose(filtered.reshape(tr_dev, shots, window), (1, 0, 2))
    outgoing = jnp.concatenate([outgoing, labels], axis=1)
    received = lax.all_to_all(outgoing, "shot", 0, 0, tiled=True)
    rows = received[:, :tr_dev].reshape(shots * tr_dev, window)
    cells = received[:, tr_dev:].reshape(shots, label_rows * window)[:, :tr_dev]
    cells = cells.reshape(shots * tr_dev).astype(jnp.int32)

    fold = jnp.sum((cells[:, None] == cells[None, :]).astype(jnp.float32), axis=1)
    scale = 1.0 / jnp.maximum(fold, 1.0)
    stacked = stack_rows(rows, cells, scale, off_dev * bin_count)
    stacked = stacked.reshape(off_dev, bin_count, window)

    ends = off_count - 1
    head = stacked[:reach]
    tail = stacked[off_dev - reach :]
    before = lax.ppermute(tail, "off", [(i, i + 1) for i in range(ends)])
    after = lax.ppermute(head, "off", [(i + 1, i) for i in range(ends)])
    return offset_mix(before, stacked, after, filter_off)


def solution(mesh):
    return jax.shard_map(
        body,
        mesh=mesh,
        in_specs=(P(("shot", "off"), None), P(("shot", "off")), P(("shot", "off")), P(), P(), P()),
        out_specs=P("off", "shot", None),
        check_vma=False,
    )
```

```python
import functools

import jax
import jax.numpy as jnp
from jax import lax
from jax.sharding import PartitionSpec as P
from jax.experimental import pallas as pl
from jax.experimental.pallas import tpu as pltpu

OFFC = 80


def tap_table(filter_time, width_in, width_out):
    inner = jnp.arange(width_in, dtype=jnp.int32)[:, None]
    outer = jnp.arange(width_out, dtype=jnp.int32)[None, :]
    distance = inner - outer
    taps = jnp.arange(filter_time.shape[0], dtype=jnp.int32)
    matches = distance[:, :, None] == taps[None, None, :]
    return jnp.sum(jnp.where(matches, filter_time[None, None, :], 0.0), axis=2)


def block_filter(data, filter_time):
    reach = filter_time.shape[0] // 2
    block_width = 128
    leading = data.shape[:-1]
    samples = data.shape[-1]
    blocks = data.reshape(leading + (samples // block_width, block_width))
    zeroes = jnp.zeros(leading + (1, reach), jnp.float32)
    before = jnp.concatenate([zeroes, blocks[..., :-1, block_width - reach :]], axis=-2)
    after = jnp.concatenate([blocks[..., 1:, :reach], zeroes], axis=-2)
    extended = jnp.concatenate([before, blocks, after], axis=-1)
    table = tap_table(filter_time, block_width + 2 * reach, block_width)
    result = jnp.einsum("...ki,io->...ko", extended, table, precision=lax.Precision.HIGHEST)
    return result.reshape(leading + (samples,))


def mix_class(taps, count, reach, filter_ref, before_ref, own_ref, after_ref, c):
    def plane(e):
        if e < reach:
            return before_ref[e]
        if e < reach + count:
            return own_ref[e - reach]
        return after_ref[e - reach - count]

    acc = filter_ref[0] * plane(c)
    for k in range(1, taps):
        acc = acc + filter_ref[k] * plane(c + k)
    return acc.T


def inner_kernel(taps, count, reach, filter_ref, own_ref, out_ref):
    for c in range(reach, count - reach):
        out_ref[c] = mix_class(taps, count, reach, filter_ref, None, own_ref, None, c)


def edge_kernel(taps, count, reach, filter_ref, before_ref, own_ref, after_ref, _, out_ref):
    step = pl.program_id(2)
    edges = list(range(reach)) + list(range(count - reach, count))
    for slot, c in enumerate(edges):
        @pl.when(step == slot)
        def _():
            out_ref[0] = mix_class(taps, count, reach, filter_ref, before_ref, own_ref, after_ref, c)


def offset_mix(before, own, after, filter_off):
    taps = filter_off.shape[0]
    count, rows, cols = own.shape
    reach = before.shape[0]
    if rows % 128 or cols % 128 or count < 2 * reach:
        ext = jnp.concatenate([before, own, after], axis=0)
        mixed = filter_off[0] * ext[0:count]
        for k in range(1, taps):
            mixed = mixed + filter_off[k] * ext[k : k + count]
        return jnp.transpose(mixed, (0, 2, 1))
    tile = 128
    inner = pl.pallas_call(
        functools.partial(inner_kernel, taps, count, reach),
        grid=(rows // tile, cols // tile),
        in_specs=[
            pl.BlockSpec(memory_space=pltpu.SMEM),
            pl.BlockSpec((count, tile, tile), lambda i, j: (0, i, j)),
        ],
        out_specs=pl.BlockSpec((count, tile, tile), lambda i, j: (0, j, i)),
        out_shape=jax.ShapeDtypeStruct((count, cols, rows), jnp.float32),
    )(filter_off, own)
    shift = count - 2 * reach
    return pl.pallas_call(
        functools.partial(edge_kernel, taps, count, reach),
        grid=(rows // tile, cols // tile, 2 * reach),
        in_specs=[
            pl.BlockSpec(memory_space=pltpu.SMEM),
            pl.BlockSpec((reach, tile, tile), lambda i, j, e: (0, i, j)),
            pl.BlockSpec((count, tile, tile), lambda i, j, e: (0, i, j)),
            pl.BlockSpec((reach, tile, tile), lambda i, j, e: (0, i, j)),
            pl.BlockSpec(memory_space=pl.ANY),
        ],
        out_specs=pl.BlockSpec((1, tile, tile), lambda i, j, e: (e + (e >= reach) * shift, j, i)),
        out_shape=jax.ShapeDtypeStruct((count, cols, rows), jnp.float32),
        input_output_aliases={4: 0},
    )(filter_off, before, own, after, inner)


def scatter_kernel(count, cell_ref, scale_ref, rows_ref, out_ref):
    out_ref[...] = jnp.zeros(out_ref.shape, jnp.float32)

    def step(i, carry):
        start = pl.multiple_of(i * 8, 8)
        tile = rows_ref[pl.ds(start, 8), :]
        for k in range(8):
            x = cell_ref[start + k]
            out_ref[pl.ds(x, 1), :] += tile[k : k + 1, :] * scale_ref[start + k]
        return carry

    lax.fori_loop(0, count // 8, step, 0)


def stack_rows(rows, cells, scale, segments):
    count, width = rows.shape
    if width % 128 or count % 8:
        return jax.ops.segment_sum(rows * scale[:, None], cells, num_segments=segments)
    return pl.pallas_call(
        functools.partial(scatter_kernel, count),
        in_specs=[
            pl.BlockSpec(memory_space=pltpu.SMEM),
            pl.BlockSpec(memory_space=pltpu.SMEM),
            pl.BlockSpec(memory_space=pltpu.VMEM),
        ],
        out_specs=pl.BlockSpec(memory_space=pltpu.VMEM),
        out_shape=jax.ShapeDtypeStruct((segments, width), jnp.float32),
    )(cells, scale, rows)


def body(traces, cmp_bin, offset_class, bin_rank, filter_off, filter_time):
    shots = lax.axis_size("shot")
    off_count = lax.axis_size("off")
    off_dev = OFFC // off_count
    first_class = lax.axis_index("off") * off_dev
    bin_count = bin_rank.shape[0]
    tr_dev, samples = traces.shape
    window = samples // shots
    reach = filter_off.shape[0] // 2

    matches = cmp_bin[:, None] == jnp.arange(bin_count, dtype=jnp.int32)[None, :]
    place = jnp.sum(jnp.where(matches, bin_rank[None, :], 0), axis=1)
    cell = (offset_class - first_class) * bin_count + place
    label_rows = -(-tr_dev // window)
    labels = jnp.pad(cell.astype(jnp.float32), (0, label_rows * window - tr_dev))
    labels = jnp.broadcast_to(labels.reshape(1, label_rows, window), (shots, label_rows, window))

    filtered = block_filter(traces, filter_time)
    outgoing = jnp.transpose(filtered.reshape(tr_dev, shots, window), (1, 0, 2))
    outgoing = jnp.concatenate([outgoing, labels], axis=1)
    received = lax.all_to_all(outgoing, "shot", 0, 0, tiled=True)
    rows = received[:, :tr_dev].reshape(shots * tr_dev, window)
    cells = received[:, tr_dev:].reshape(shots, label_rows * window)[:, :tr_dev]
    cells = cells.reshape(shots * tr_dev).astype(jnp.int32)

    fold = jnp.sum((cells[:, None] == cells[None, :]).astype(jnp.float32), axis=1)
    scale = 1.0 / jnp.maximum(fold, 1.0)
    stacked = stack_rows(rows, cells, scale, off_dev * bin_count)
    stacked = stacked.reshape(off_dev, bin_count, window)

    ends = off_count - 1
    head = stacked[:reach]
    tail = stacked[off_dev - reach :]
    before = lax.ppermute(tail, "off", [(i, i + 1) for i in range(ends)])
    after = lax.ppermute(head, "off", [(i + 1, i) for i in range(ends)])
    return offset_mix(before, stacked, after, filter_off)


def solution(mesh):
    return jax.shard_map(
        body,
        mesh=mesh,
        in_specs=(P(("shot", "off"), None), P(("shot", "off")), P(("shot", "off")), P(), P(), P()),
        out_specs=P("off", "shot", None),
        check_vma=False,
    )
```

```python
import functools

import jax
import jax.numpy as jnp
from jax import lax
from jax.sharding import PartitionSpec as P
from jax.experimental import pallas as pl
from jax.experimental.pallas import tpu as pltpu

OFFC = 80


def tap_table(filter_time, width_in, width_out):
    inner = jnp.arange(width_in, dtype=jnp.int32)[:, None]
    outer = jnp.arange(width_out, dtype=jnp.int32)[None, :]
    distance = inner - outer
    taps = jnp.arange(filter_time.shape[0], dtype=jnp.int32)
    matches = distance[:, :, None] == taps[None, None, :]
    return jnp.sum(jnp.where(matches, filter_time[None, None, :], 0.0), axis=2)


def block_filter(data, filter_time):
    reach = filter_time.shape[0] // 2
    block_width = 128
    leading = data.shape[:-1]
    samples = data.shape[-1]
    blocks = data.reshape(leading + (samples // block_width, block_width))
    zeroes = jnp.zeros(leading + (1, reach), jnp.float32)
    before = jnp.concatenate([zeroes, blocks[..., :-1, block_width - reach :]], axis=-2)
    after = jnp.concatenate([blocks[..., 1:, :reach], zeroes], axis=-2)
    extended = jnp.concatenate([before, blocks, after], axis=-1)
    table = tap_table(filter_time, block_width + 2 * reach, block_width)
    result = jnp.einsum("...ki,io->...ko", extended, table, precision=lax.Precision.HIGHEST)
    return result.reshape(leading + (samples,))


def mix_class(taps, count, reach, filter_ref, before_ref, own_ref, after_ref, c):
    def plane(e):
        if e < reach:
            return before_ref[e]
        if e < reach + count:
            return own_ref[e - reach]
        return after_ref[e - reach - count]

    acc = filter_ref[0] * plane(c)
    for k in range(1, taps):
        acc = acc + filter_ref[k] * plane(c + k)
    return acc.T


def inner_kernel(taps, count, reach, filter_ref, own_ref, out_ref):
    for c in range(reach, count - reach):
        out_ref[c] = mix_class(taps, count, reach, filter_ref, None, own_ref, None, c)


def edge_kernel(taps, count, reach, filter_ref, before_ref, own_ref, after_ref, _, out_ref):
    step = pl.program_id(2)
    edges = list(range(reach)) + list(range(count - reach, count))
    for slot, c in enumerate(edges):
        @pl.when(step == slot)
        def _():
            out_ref[0] = mix_class(taps, count, reach, filter_ref, before_ref, own_ref, after_ref, c)


def offset_mix(before, own, after, filter_off):
    taps = filter_off.shape[0]
    count, rows, cols = own.shape
    reach = before.shape[0]
    if rows % 128 or cols % 128 or count < 2 * reach:
        ext = jnp.concatenate([before, own, after], axis=0)
        mixed = filter_off[0] * ext[0:count]
        for k in range(1, taps):
            mixed = mixed + filter_off[k] * ext[k : k + count]
        return jnp.transpose(mixed, (0, 2, 1))
    tile = 128
    inner = pl.pallas_call(
        functools.partial(inner_kernel, taps, count, reach),
        grid=(rows // tile, cols // tile),
        in_specs=[
            pl.BlockSpec(memory_space=pltpu.SMEM),
            pl.BlockSpec((count, tile, tile), lambda i, j: (0, i, j)),
        ],
        out_specs=pl.BlockSpec((count, tile, tile), lambda i, j: (0, j, i)),
        out_shape=jax.ShapeDtypeStruct((count, cols, rows), jnp.float32),
    )(filter_off, own)
    shift = count - 2 * reach
    tile = 256 if rows % 256 == 0 and cols % 256 == 0 else 128
    return pl.pallas_call(
        functools.partial(edge_kernel, taps, count, reach),
        grid=(rows // tile, cols // tile, 2 * reach),
        in_specs=[
            pl.BlockSpec(memory_space=pltpu.SMEM),
            pl.BlockSpec((reach, tile, tile), lambda i, j, e: (0, i, j)),
            pl.BlockSpec((count, tile, tile), lambda i, j, e: (0, i, j)),
            pl.BlockSpec((reach, tile, tile), lambda i, j, e: (0, i, j)),
            pl.BlockSpec(memory_space=pl.ANY),
        ],
        out_specs=pl.BlockSpec((1, tile, tile), lambda i, j, e: (e + (e >= reach) * shift, j, i)),
        out_shape=jax.ShapeDtypeStruct((count, cols, rows), jnp.float32),
        input_output_aliases={4: 0},
    )(filter_off, before, own, after, inner)


def scatter_kernel(count, cell_ref, scale_ref, rows_ref, out_ref):
    out_ref[...] = jnp.zeros(out_ref.shape, jnp.float32)

    def step(i, carry):
        start = pl.multiple_of(i * 8, 8)
        tile = rows_ref[pl.ds(start, 8), :]
        for k in range(8):
            x = cell_ref[start + k]
            out_ref[pl.ds(x, 1), :] += tile[k : k + 1, :] * scale_ref[start + k]
        return carry

    lax.fori_loop(0, count // 8, step, 0)


def stack_rows(rows, cells, scale, segments):
    count, width = rows.shape
    if width % 128 or count % 8:
        return jax.ops.segment_sum(rows * scale[:, None], cells, num_segments=segments)
    return pl.pallas_call(
        functools.partial(scatter_kernel, count),
        in_specs=[
            pl.BlockSpec(memory_space=pltpu.SMEM),
            pl.BlockSpec(memory_space=pltpu.SMEM),
            pl.BlockSpec(memory_space=pltpu.VMEM),
        ],
        out_specs=pl.BlockSpec(memory_space=pltpu.VMEM),
        out_shape=jax.ShapeDtypeStruct((segments, width), jnp.float32),
    )(cells, scale, rows)


def body(traces, cmp_bin, offset_class, bin_rank, filter_off, filter_time):
    shots = lax.axis_size("shot")
    off_count = lax.axis_size("off")
    off_dev = OFFC // off_count
    first_class = lax.axis_index("off") * off_dev
    bin_count = bin_rank.shape[0]
    tr_dev, samples = traces.shape
    window = samples // shots
    reach = filter_off.shape[0] // 2

    matches = cmp_bin[:, None] == jnp.arange(bin_count, dtype=jnp.int32)[None, :]
    place = jnp.sum(jnp.where(matches, bin_rank[None, :], 0), axis=1)
    cell = (offset_class - first_class) * bin_count + place
    label_rows = -(-tr_dev // window)
    labels = jnp.pad(cell.astype(jnp.float32), (0, label_rows * window - tr_dev))
    labels = jnp.broadcast_to(labels.reshape(1, label_rows, window), (shots, label_rows, window))

    filtered = block_filter(traces, filter_time)
    outgoing = jnp.transpose(filtered.reshape(tr_dev, shots, window), (1, 0, 2))
    outgoing = jnp.concatenate([outgoing, labels], axis=1)
    received = lax.all_to_all(outgoing, "shot", 0, 0, tiled=True)
    rows = received[:, :tr_dev].reshape(shots * tr_dev, window)
    cells = received[:, tr_dev:].reshape(shots, label_rows * window)[:, :tr_dev]
    cells = cells.reshape(shots * tr_dev).astype(jnp.int32)

    fold = jnp.sum((cells[:, None] == cells[None, :]).astype(jnp.float32), axis=1)
    scale = 1.0 / jnp.maximum(fold, 1.0)
    stacked = stack_rows(rows, cells, scale, off_dev * bin_count)
    stacked = stacked.reshape(off_dev, bin_count, window)

    ends = off_count - 1
    head = stacked[:reach]
    tail = stacked[off_dev - reach :]
    before = lax.ppermute(tail, "off", [(i, i + 1) for i in range(ends)])
    after = lax.ppermute(head, "off", [(i + 1, i) for i in range(ends)])
    return offset_mix(before, stacked, after, filter_off)


def solution(mesh):
    return jax.shard_map(
        body,
        mesh=mesh,
        in_specs=(P(("shot", "off"), None), P(("shot", "off")), P(("shot", "off")), P(), P(), P()),
        out_specs=P("off", "shot", None),
        check_vma=False,
    )
```

```python
import functools

import jax
import jax.numpy as jnp
from jax import lax
from jax.sharding import PartitionSpec as P
from jax.experimental import pallas as pl
from jax.experimental.pallas import tpu as pltpu

OFFC = 80


def tap_table(filter_time, width_in, width_out):
    inner = jnp.arange(width_in, dtype=jnp.int32)[:, None]
    outer = jnp.arange(width_out, dtype=jnp.int32)[None, :]
    distance = inner - outer
    taps = jnp.arange(filter_time.shape[0], dtype=jnp.int32)
    matches = distance[:, :, None] == taps[None, None, :]
    return jnp.sum(jnp.where(matches, filter_time[None, None, :], 0.0), axis=2)


def block_filter(data, filter_time):
    reach = filter_time.shape[0] // 2
    block_width = 128
    leading = data.shape[:-1]
    samples = data.shape[-1]
    blocks = data.reshape(leading + (samples // block_width, block_width))
    zeroes = jnp.zeros(leading + (1, reach), jnp.float32)
    before = jnp.concatenate([zeroes, blocks[..., :-1, block_width - reach :]], axis=-2)
    after = jnp.concatenate([blocks[..., 1:, :reach], zeroes], axis=-2)
    extended = jnp.concatenate([before, blocks, after], axis=-1)
    table = tap_table(filter_time, block_width + 2 * reach, block_width)
    result = jnp.einsum("...ki,io->...ko", extended, table, precision=lax.Precision.HIGHEST)
    return result.reshape(leading + (samples,))


def mix_class(taps, count, reach, filter_ref, before_ref, own_ref, after_ref, c):
    def plane(e):
        if e < reach:
            return before_ref[e]
        if e < reach + count:
            return own_ref[e - reach]
        return after_ref[e - reach - count]

    acc = filter_ref[0] * plane(c)
    for k in range(1, taps):
        acc = acc + filter_ref[k] * plane(c + k)
    return acc.T


def inner_kernel(taps, count, reach, filter_ref, own_ref, out_ref):
    for c in range(reach, count - reach):
        out_ref[c] = mix_class(taps, count, reach, filter_ref, None, own_ref, None, c)


def edge_kernel(taps, count, reach, filter_ref, before_ref, own_ref, after_ref, _, out_ref):
    step = pl.program_id(2)
    edges = list(range(reach)) + list(range(count - reach, count))
    for slot, c in enumerate(edges):
        @pl.when(step == slot)
        def _():
            out_ref[0] = mix_class(taps, count, reach, filter_ref, before_ref, own_ref, after_ref, c)


def offset_mix(before, own, after, filter_off):
    taps = filter_off.shape[0]
    count, rows, cols = own.shape
    reach = before.shape[0]
    if rows % 128 or cols % 128 or count < 2 * reach:
        ext = jnp.concatenate([before, own, after], axis=0)
        mixed = filter_off[0] * ext[0:count]
        for k in range(1, taps):
            mixed = mixed + filter_off[k] * ext[k : k + count]
        return jnp.transpose(mixed, (0, 2, 1))
    tile = 128
    inner = pl.pallas_call(
        functools.partial(inner_kernel, taps, count, reach),
        grid=(rows // tile, cols // tile),
        in_specs=[
            pl.BlockSpec(memory_space=pltpu.SMEM),
            pl.BlockSpec((count, tile, tile), lambda i, j: (0, i, j)),
        ],
        out_specs=pl.BlockSpec((count, tile, tile), lambda i, j: (0, j, i)),
        out_shape=jax.ShapeDtypeStruct((count, cols, rows), jnp.float32),
    )(filter_off, own)
    shift = count - 2 * reach
    tile = 256 if rows % 256 == 0 and cols % 256 == 0 else 128
    return pl.pallas_call(
        functools.partial(edge_kernel, taps, count, reach),
        grid=(rows // tile, cols // tile, 2 * reach),
        in_specs=[
            pl.BlockSpec(memory_space=pltpu.SMEM),
            pl.BlockSpec((reach, tile, tile), lambda i, j, e: (0, i, j)),
            pl.BlockSpec((count, tile, tile), lambda i, j, e: (0, i, j)),
            pl.BlockSpec((reach, tile, tile), lambda i, j, e: (0, i, j)),
            pl.BlockSpec(memory_space=pl.ANY),
        ],
        out_specs=pl.BlockSpec((1, tile, tile), lambda i, j, e: (e + (e >= reach) * shift, j, i)),
        out_shape=jax.ShapeDtypeStruct((count, cols, rows), jnp.float32),
        input_output_aliases={4: 0},
    )(filter_off, before, own, after, inner)


def scatter_kernel(count, tr_dev, cell_ref, scale_ref, rows_ref, out_ref):
    out_ref[...] = jnp.zeros(out_ref.shape, jnp.float32)

    def step(i, carry):
        start = pl.multiple_of(i * 8, 8)
        src = start // tr_dev
        local = pl.multiple_of(start - src * tr_dev, 8)
        tile = rows_ref[src, pl.ds(local, 8), :]
        for k in range(8):
            x = cell_ref[start + k]
            out_ref[pl.ds(x, 1), :] += tile[k : k + 1, :] * scale_ref[start + k]
        return carry

    lax.fori_loop(0, count // 8, step, 0)


def stack_rows(received, cells, scale, segments):
    shots, _, width = received.shape
    count = cells.shape[0]
    tr_dev = count // shots
    if width % 128 or tr_dev % 8:
        rows = received[:, :tr_dev].reshape(count, width)
        return jax.ops.segment_sum(rows * scale[:, None], cells, num_segments=segments)
    return pl.pallas_call(
        functools.partial(scatter_kernel, count, tr_dev),
        in_specs=[
            pl.BlockSpec(memory_space=pltpu.SMEM),
            pl.BlockSpec(memory_space=pltpu.SMEM),
            pl.BlockSpec(memory_space=pltpu.VMEM),
        ],
        out_specs=pl.BlockSpec(memory_space=pltpu.VMEM),
        out_shape=jax.ShapeDtypeStruct((segments, width), jnp.float32),
    )(cells, scale, received)


def body(traces, cmp_bin, offset_class, bin_rank, filter_off, filter_time):
    shots = lax.axis_size("shot")
    off_count = lax.axis_size("off")
    off_dev = OFFC // off_count
    first_class = lax.axis_index("off") * off_dev
    bin_count = bin_rank.shape[0]
    tr_dev, samples = traces.shape
    window = samples // shots
    reach = filter_off.shape[0] // 2

    matches = cmp_bin[:, None] == jnp.arange(bin_count, dtype=jnp.int32)[None, :]
    place = jnp.sum(jnp.where(matches, bin_rank[None, :], 0), axis=1)
    cell = (offset_class - first_class) * bin_count + place
    label_rows = -(-tr_dev // window)
    labels = jnp.pad(cell.astype(jnp.float32), (0, label_rows * window - tr_dev))
    labels = jnp.broadcast_to(labels.reshape(1, label_rows, window), (shots, label_rows, window))

    filtered = block_filter(traces, filter_time)
    outgoing = jnp.transpose(filtered.reshape(tr_dev, shots, window), (1, 0, 2))
    outgoing = jnp.concatenate([outgoing, labels], axis=1)
    received = lax.all_to_all(outgoing, "shot", 0, 0, tiled=True)
    cells = received[:, tr_dev:].reshape(shots, label_rows * window)[:, :tr_dev]
    cells = cells.reshape(shots * tr_dev).astype(jnp.int32)

    fold = jnp.sum((cells[:, None] == cells[None, :]).astype(jnp.float32), axis=1)
    scale = 1.0 / jnp.maximum(fold, 1.0)
    stacked = stack_rows(received, cells, scale, off_dev * bin_count)
    stacked = stacked.reshape(off_dev, bin_count, window)

    ends = off_count - 1
    head = stacked[:reach]
    tail = stacked[off_dev - reach :]
    before = lax.ppermute(tail, "off", [(i, i + 1) for i in range(ends)])
    after = lax.ppermute(head, "off", [(i + 1, i) for i in range(ends)])
    return offset_mix(before, stacked, after, filter_off)


def solution(mesh):
    return jax.shard_map(
        body,
        mesh=mesh,
        in_specs=(P(("shot", "off"), None), P(("shot", "off")), P(("shot", "off")), P(), P(), P()),
        out_specs=P("off", "shot", None),
        check_vma=False,
    )
```
